256 devices in a mesh: ctx: 32 (over y, x, core), head: 8 (over z).
Axes of the slice: x: 4, y: 4, z: 8, core: 2. Of those that a mesh axis runs over, the one named last changes fastest.
Arguments:
- queries: bfloat16 [8192, 4096], P('ctx', 'head'), may hold values from -6 to 6
- key_rows: bfloat16 [8192, 4096], P('ctx', 'head'), may hold values from -6 to 6
- values: bfloat16 [8192, 4096], P('ctx', 'head'), may hold values from -6 to 6
- log_decay: float32 [8192, 32], P('ctx', 'head'), may hold values from 0 to 1, as said below
- head_gain: bfloat16 [4096], P('head'), may hold values from 0.099609375 to 1.8984375
- out_weight: bfloat16 [3072, 4096], P('ctx', 'head'), may hold values from -0.09375 to 0.09375
- residual: bfloat16 [8192, 3072], P('ctx', 'head'), may hold values from -6 to 6
- norm_gain: bfloat16 [3072], P('head'), may hold values from 0.099609375 to 1.8984375
- router: bfloat16 [3072, 32], replicated, may hold values from -0.21875 to 0.21875
- expert_ids: int32 [8192, 2], P('ctx'), may hold values from 0 to 31, all different within a row; in each aligned block of 256 rows (0 to 255, 256 to 511, ...) at most 24 rows name the same one
- gate_weight: bfloat16 [32, 3072, 5120], P('ctx', None, 'head'), may hold values from -0.109375 to 0.109375
- up_weight: bfloat16 [32, 3072, 5120], P('ctx', None, 'head'), may hold values from -0.109375 to 0.109375
- down_weight: bfloat16 [32, 5120, 3072], P('ctx', 'head'), may hold values from -0.125 to 0.125
Outputs:
- layer_out: float32 [8192, 3072], P('ctx', 'head')
The draws below stay inside these ranges and needn't reach their ends.
Inputs may be any that keep to these rules, and one draw needn't show every extreme that they name: `log_decay`: amounts by which a head's state decays at a position: the state is multiplied by exp(-value). `expert_ids`: each row names 2 different experts; among the rows of one block of 256 positions no expert is named more than 24 times, a bound that some block reaches.
All inputs are finite; a program needn't handle non-finite values.
Results may differ from the reference program's by a relative error of at most 0.007.
Values may be sent and summed in bfloat16 or wider, within the bound.
No kernel may reach another device: no remote copies, remote signals or barrier semaphores. Data moves between devices by JAX's collectives and lax.ppermute only.
A program may use at most 128 MiB of HBM per device.

```python
import math
import jax
import jax.numpy as jnp
import numpy as np
from jax import lax

D = 3072
HEADS = 32
HEAD_DIM = 128
FF = 5120
TOP = 2
TOK_DEV = 256
SEQUENCE_TOKENS = 8192
EXPERTS = 32
CAP = 24
FF_DEV = 640


def draw_log_decay(key, part):
    keys = jax.random.split(key, 6)
    fast_share = 0.5
    fast = jax.random.bernoulli(keys[0], fast_share, (HEADS,))
    fast_rate = jnp.exp(jax.random.uniform(keys[1], (HEADS,), jnp.float32, jnp.log(1.0 / 50.0), jnp.log(1.0 / 30.0)))
    slow_rate = jnp.exp(jax.random.uniform(keys[2], (HEADS,), jnp.float32, jnp.log(0.05), jnp.log(0.3))) / SEQUENCE_TOKENS
    baseline_value = jnp.where(fast, fast_rate, slow_rate)
    coarse_estimate = jax.random.uniform(keys[3], (SEQUENCE_TOKENS, HEADS), jnp.float32, 0.5, 1.5)
    slot_positions = jax.random.randint(keys[4], (3,), 0, SEQUENCE_TOKENS)
    expert_surge = jnp.any(jnp.arange(SEQUENCE_TOKENS)[:, None] == slot_positions[None, :], axis=1).astype(jnp.float32)
    training_loss = jax.random.uniform(keys[5], (HEADS,), jnp.float32, 0.2, 0.45)
    return baseline_value[None, :] * coarse_estimate - expert_surge[:, None] * jnp.log(1.0 - training_loss)[None, :]


def with_spikes(entries, stream_key, source, target, shards_of, factor):
    def block_of(axis_at):
        return (jnp.arange(entries.shape[axis_at]) // (entries.shape[axis_at] // shards_of)).reshape((-1,) + (1,) * (entries.ndim - 1 - axis_at))

    one_side = jax.random.permutation(stream_key, shards_of)[block_of(target)]
    far = (block_of(target) + shards_of // 2) % shards_of
    return jnp.where((block_of(source) == one_side) | (block_of(source) == far), factor * entries, entries)


def block_levels(own_key, dims, cuts, least, high):
    factor_of = 1.0
    for dim, shards_of in cuts:
        steps = jax.random.uniform(jax.random.fold_in(jax.random.fold_in(own_key, 6), dim), (shards_of,), jnp.float32, least / len(cuts), high / len(cuts))
        factor_of = factor_of * jnp.repeat(jnp.exp(steps), dims[dim] // shards_of).reshape((-1,) + (1,) * (len(dims) - 1 - dim))
    return factor_of


def deal_out(stream_key, own, number, rows, amount, top, bound, skew):
    sequence = jax.random.permutation(stream_key, amount)
    packed, ordinary = load_shares(amount, rows * top, bound, skew, True), load_shares(amount, rows * top, bound, skew, False)
    places = jnp.arange(amount)

    def named(lengths, rotation):
        used = int((lengths > 0).sum())
        fixed = max(1, used // 4)
        shifted = fixed + (places - fixed + rotation * (used - fixed)) % max(1, amount - fixed)
        return jnp.zeros((amount,), jnp.int32).at[sequence[jnp.where(places < fixed, places, shifted)]].set(jnp.asarray(lengths, jnp.int32))

    lengths = jnp.where(number % 4 == 0, named(packed, number // 4), named(ordinary, number - number // 4 - 1))
    mixed = jax.random.permutation(jax.random.fold_in(own, 3), amount)
    source_of, sink = mixed[0:amount // 2 * 2:2], mixed[1:amount // 2 * 2:2]
    room = jnp.minimum(lengths[source_of] - 1, bound - lengths[sink]) // 2
    room = jnp.where((source_of == sequence[0]) | (sink == sequence[0]) | (lengths[sink] == 0), 0, jnp.maximum(room, 0))
    shifted = jax.random.randint(jax.random.fold_in(own, 4), (amount // 2,), 0, 1 << 20) % (room + 1)
    lengths = lengths.at[source_of].add(-shifted).at[sink].add(shifted)
    items = jnp.searchsorted(jnp.cumsum(lengths), jnp.arange(rows * top), side="right").astype(jnp.int32)
    table = items.reshape(top, rows).T
    table = table[jax.random.permutation(jax.random.fold_in(own, 1), rows)]
    rotation = jax.random.randint(jax.random.fold_in(own, 2), (rows, 1), 0, top)
    return jnp.take_along_axis(table, (jnp.arange(top)[None, :] + rotation) % top, axis=1)


def load_shares(amount, total, limit, lean, full):
    loads = [(1 << 20) // math.isqrt(rank ** lean) + 1 for rank in range(1, amount + 1)]
    largest = limit if full else min(limit, max(-(-total // amount), total * loads[0] // sum(loads)))
    least = 1 if total - largest >= amount - 1 else 0
    holding, rest = [largest] + [least] * (amount - 1), total - largest - least * (amount - 1)
    while rest > 0:
        free = [i for i in range(1, amount) if holding[i] < largest] or [i for i in range(1, amount) if holding[i] < limit]
        whole, remaining = sum([loads[i] for i in free]), rest
        for i in free:
            extra = min(limit - holding[i], max(1, remaining * loads[i] // whole), rest)
            holding[i] = holding[i] + extra
            rest = rest - extra
    return np.array(holding)


def gaussian(own_key, dims, deviation, limit, pieces=(), kind=jnp.bfloat16):
    values = jax.random.normal(own_key, dims, jnp.float32) * deviation
    if len(pieces) > 0:
        values = block_levels(own_key, dims, pieces, -0.22, 0.18) * values
    return jnp.clip(values, min=-limit, max=limit).astype(kind)


def gaussian_with(own_key, shape, scale, bound, cuts, heavy, kind=jnp.bfloat16):
    values = scale * jax.random.normal(own_key, shape, jnp.float32)
    if cuts:
        values = values * block_levels(own_key, shape, cuts, -0.22, 0.18)
    return jnp.clip(with_spikes(values, jax.random.fold_in(own_key, 3), *heavy), -bound, bound).astype(kind)


def setup_inputs(seed: int = 0) -> dict:
    splits = jax.random.split(jax.random.key(seed), 14)
    queries = gaussian(splits[0], (SEQUENCE_TOKENS, HEADS * HEAD_DIM), 1.0, 6.0, ((0, 32), (1, 8)))
    key_rows = gaussian(splits[1], (SEQUENCE_TOKENS, HEADS * HEAD_DIM), 1.0, 6.0, ((0, 32), (1, 8)))
    values = gaussian(splits[2], (SEQUENCE_TOKENS, HEADS * HEAD_DIM), 1.0, 6.0, ((0, 32), (1, 8)))
    log_decay = draw_log_decay(jax.random.fold_in(splits[13], 71), 0)
    head_gain = jnp.clip(1.0 + 0.18 * jax.random.normal(splits[4], (HEADS * HEAD_DIM,), jnp.float32), 0.099609375, 1.8984375).astype(jnp.bfloat16)
    out_weight = gaussian(splits[5], (D, HEADS * HEAD_DIM), (HEADS * HEAD_DIM) ** -0.5, 0.09375, ((0, 32), (1, 8)))
    residual = gaussian(splits[6], (SEQUENCE_TOKENS, D), 1.0, 6.0, ((0, 32), (1, 8)))
    norm_gain = jnp.clip(1.0 + 0.18 * jax.random.normal(splits[7], (D,), jnp.float32), 0.099609375, 1.8984375).astype(jnp.bfloat16)
    router = gaussian(splits[8], (D, EXPERTS), (D // 4) ** -0.5, 0.21875)
    expert_ids_keys = jax.random.split(jax.random.fold_in(splits[9], 1), SEQUENCE_TOKENS // TOK_DEV)
    expert_ids_turns = jax.random.permutation(jax.random.fold_in(splits[9], 3), SEQUENCE_TOKENS // TOK_DEV)
    expert_ids = jax.vmap(lambda own, number: deal_out(jax.random.fold_in(splits[9], 2), own, number, TOK_DEV, EXPERTS, TOP, CAP, 2))(expert_ids_keys, expert_ids_turns).reshape((SEQUENCE_TOKENS, TOP))
    gate_weight = gaussian(splits[10], (EXPERTS, D, FF), D ** -0.5, 0.109375, ((0, 32), (2, 8)))
    up_weight = gaussian(splits[11], (EXPERTS, D, FF), D ** -0.5, 0.109375, ((0, 32), (2, 8)))
    down_weight = gaussian_with(splits[12], (EXPERTS, FF, D), FF ** -0.5, 0.125, ((0, 32), (1, 8)), (1, 2, 8, 2.0))
    return {"queries": queries, "key_rows": key_rows, "values": values, "log_decay": log_decay, "head_gain": head_gain, "out_weight": out_weight, "residual": residual, "norm_gain": norm_gain, "router": router, "expert_ids": expert_ids, "gate_weight": gate_weight, "up_weight": up_weight, "down_weight": down_weight}


HIGH = lax.Precision.HIGHEST
EPSILON = 1e-05

def lightning_block(state, block):
    query_heads, key_heads, value_heads, decay = block
    cumulative = jnp.cumsum(decay, axis=0)
    query_wide = query_heads.astype(jnp.float32)
    key_wide = key_heads.astype(jnp.float32)
    value_wide = value_heads.astype(jnp.float32)
    scores = jnp.einsum('thd,jhd->htj', query_wide, key_wide, precision=HIGH)
    causal = jnp.arange(TOK_DEV)[:, None] >= jnp.arange(TOK_DEV)[None, :]
    gap = cumulative.T[:, :, None] - cumulative.T[:, None, :]
    weight = jnp.where(causal[None], jnp.exp(-jnp.where(causal[None], gap, 0.0)), 0.0)
    weighted = lax.optimization_barrier((scores * weight).astype(jnp.bfloat16)).astype(jnp.float32)
    inner = jnp.einsum('htj,jhd->thd', weighted, value_wide, precision=HIGH)
    query_decayed = query_wide * jnp.exp(-cumulative)[:, :, None]
    outer = jnp.einsum('thd,hde->the', query_decayed, state, precision=HIGH)
    tail = jnp.exp(cumulative - cumulative[-1:])
    local_state = jnp.einsum('jhd,jhe->hde', key_wide * tail[:, :, None], value_wide, precision=HIGH)
    new_state = jnp.exp(-cumulative[-1])[:, None, None] * state + local_state
    return (new_state, inner + outer)

def shard_slots(ids):
    flat_ids = ids.reshape(-1).astype(jnp.int32)
    onehot = (flat_ids[:, None] == jnp.arange(EXPERTS, dtype=jnp.int32)[None, :]).astype(jnp.int32)
    before = (jnp.cumsum(onehot, axis=0) - onehot).astype(jnp.int32)
    position = lax.optimization_barrier(jnp.sum(before * onehot, axis=1)).astype(jnp.int32)
    slot = (flat_ids * CAP + position).astype(jnp.int32)
    owner = (jnp.arange(TOK_DEV * TOP, dtype=jnp.int32) // TOP).astype(jnp.int32)
    slot_token = jnp.zeros((EXPERTS * CAP,), jnp.int32).at[slot].set(owner)
    filled = jnp.zeros((EXPERTS * CAP,), jnp.bool_).at[slot].set(True)
    return (slot, slot_token, filled)

def outgoing_rows(block_rows, tokens_at, used):
    return jnp.where(used[:, None], block_rows[tokens_at], jnp.zeros((), jnp.bfloat16))

def selected_rows(rows_all, index):
    return rows_all[index]

def run_expert(operands):
    gate_mat, up_mat, down_mat, arriving = operands
    flat = arriving.reshape(-1, D)
    gate = jnp.dot(flat, gate_mat, preferred_element_type=jnp.float32)
    up = jnp.dot(flat, up_mat, preferred_element_type=jnp.float32)
    activated = (jax.nn.silu(gate) * up).astype(jnp.bfloat16)
    total = jnp.zeros((flat.shape[0], D), jnp.float32)
    for group in range(FF // FF_DEV):
        piece = jnp.dot(activated[:, group * FF_DEV:(group + 1) * FF_DEV], down_mat[group * FF_DEV:(group + 1) * FF_DEV, :], preferred_element_type=jnp.float32)
        rounded = lax.optimization_barrier(piece.astype(jnp.bfloat16))
        total = total + rounded.astype(jnp.float32)
    return total.astype(jnp.bfloat16).reshape(arriving.shape[0], CAP, D)

def reference(queries, key_rows, values, log_decay, head_gain, out_weight, residual, norm_gain, router, expert_ids, gate_weight, up_weight, down_weight):
    shards = SEQUENCE_TOKENS // TOK_DEV

    def split_blocks(array):
        return array.reshape(shards, TOK_DEV, HEADS, HEAD_DIM)
    blocks = (split_blocks(queries), split_blocks(key_rows), split_blocks(values), log_decay.reshape(shards, TOK_DEV, HEADS))
    start = jnp.zeros((HEADS, HEAD_DIM, HEAD_DIM), jnp.float32)
    _, mixed = lax.scan(lightning_block, start, blocks)
    mixed = mixed.reshape(SEQUENCE_TOKENS, HEADS, HEAD_DIM)
    mean_sq = lax.optimization_barrier(jnp.mean(mixed * mixed, axis=-1, keepdims=True))
    gain_heads = head_gain.astype(jnp.float32).reshape(HEADS, HEAD_DIM)
    normed = (mixed * lax.rsqrt(mean_sq + EPSILON) * gain_heads).astype(jnp.bfloat16).reshape(SEQUENCE_TOKENS, HEADS * HEAD_DIM)
    stream = residual.astype(jnp.float32) + jnp.dot(normed, out_weight.T, preferred_element_type=jnp.float32)
    stream_sq = lax.optimization_barrier(jnp.mean(stream * stream, axis=-1, keepdims=True))
    moe_in = (stream * lax.rsqrt(stream_sq + EPSILON) * norm_gain.astype(jnp.float32)).astype(jnp.bfloat16)
    logits = jnp.dot(moe_in, router, preferred_element_type=jnp.float32)
    picked_mask = expert_ids[:, :, None] == jnp.arange(EXPERTS, dtype=jnp.int32)[None, None, :]
    picked = lax.optimization_barrier(jnp.sum(jnp.where(picked_mask, logits[:, None, :], 0.0), axis=-1))
    mix_weights = jax.nn.sigmoid(picked - picked[:, ::-1])
    slot, slot_token, filled = jax.vmap(shard_slots)(expert_ids.reshape(shards, TOK_DEV, TOP))
    moe_blocks = moe_in.reshape(shards, TOK_DEV, D)
    outgoing = jax.vmap(outgoing_rows)(moe_blocks, slot_token, filled).reshape(shards, EXPERTS, CAP, D)
    expert_outs = lax.map(run_expert, (gate_weight, up_weight, down_weight, jnp.swapaxes(outgoing, 0, 1)))
    returned = jnp.swapaxes(expert_outs, 0, 1).reshape(shards, EXPERTS * CAP, D)
    picked_rows = jax.vmap(selected_rows)(returned, slot).astype(jnp.float32).reshape(SEQUENCE_TOKENS, TOP, D)
    moe_out = lax.optimization_barrier(jnp.sum(picked_rows * mix_weights[:, :, None], axis=1))
    return stream + moe_out
```

```python
import jax
import jax.numpy as jnp
from jax import lax
from jax.sharding import PartitionSpec as P

HEAD_DIM = 128
TOP = 2


HIGH = lax.Precision.HIGHEST
EPSILON = 1e-05


def combine(earlier, later):
    rows = HEAD_DIM
    decay_late = later[:, rows:rows + 1, 0:1]
    state = decay_late * earlier[:, :rows] + later[:, :rows]
    decay = earlier[:, rows:rows + 1] * later[:, rows:rows + 1]
    pad = jnp.zeros((later.shape[0], later.shape[1] - rows - 1, later.shape[2]), later.dtype)
    return jnp.concatenate([state, decay, pad], axis=1)


def exclusive_scan(packed, axis):
    count, mine = lax.axis_size(axis), lax.axis_index(axis)
    rows = HEAD_DIM
    identity = jnp.zeros_like(packed).at[:, rows].set(1.0)
    window = packed
    before = identity
    shift = 1
    while shift < count:
        pairs = [(j, j + shift) for j in range(count - shift)]
        got = lax.ppermute(window, axis, pairs)
        got = jnp.where(mine >= shift, got, identity)
        before = combine(got, before)
        if 2 * shift < count:
            window = combine(got, window)
        shift *= 2
    return before[:, :rows]


def on_device(
    queries,
    key_rows,
    values,
    log_decay,
    head_gain,
    out_weight,
    residual,
    norm_gain,
    router,
    expert_ids,
    gate_weight,
    up_weight,
    down_weight,
):
    rows = queries.shape[0]
    heads_here = log_decay.shape[1]
    groups = lax.axis_size("head")
    query_heads = queries.reshape(rows, heads_here, HEAD_DIM)
    key_heads = key_rows.reshape(rows, heads_here, HEAD_DIM)
    value_heads = values.reshape(rows, heads_here, HEAD_DIM)
    cumulative = jnp.cumsum(log_decay, axis=0)
    scores = jnp.einsum("thd,jhd->htj", query_heads, key_heads, preferred_element_type=jnp.float32)
    causal = jnp.arange(rows)[:, None] >= jnp.arange(rows)[None, :]
    gap = cumulative.T[:, :, None] - cumulative.T[:, None, :]
    weight = jnp.where(causal[None], jnp.exp(-jnp.where(causal[None], gap, 0.0)), 0.0)
    weighted = (scores * weight).astype(jnp.bfloat16)
    inner = jnp.einsum("htj,jhd->thd", weighted, value_heads, preferred_element_type=jnp.float32)
    value_wide = value_heads.astype(jnp.float32)
    tail = jnp.exp(cumulative - cumulative[-1:])
    keys_tail = key_heads.astype(jnp.float32) * tail[:, :, None]
    local_state = jnp.einsum("jhd,jhe->hde", keys_tail, value_wide, precision=HIGH)
    shard_decay = jnp.exp(-cumulative[-1])
    decay_rows = jnp.broadcast_to(shard_decay[:, None, None], (heads_here, 1, HEAD_DIM))
    pad = jnp.zeros((heads_here, 7, HEAD_DIM), jnp.float32)
    packed = jnp.concatenate([local_state, decay_rows, pad], axis=1)
    incoming = exclusive_scan(packed, "ctx")
    query_decayed = query_heads.astype(jnp.float32) * jnp.exp(-cumulative)[:, :, None]
    outer = jnp.einsum("thd,hde->the", query_decayed, incoming, precision=HIGH)
    mixed = inner + outer
    mean_sq = jnp.mean(mixed * mixed, axis=-1, keepdims=True)
    gain_heads = head_gain.astype(jnp.float32).reshape(heads_here, HEAD_DIM)
    normed = (
        (mixed * lax.rsqrt(mean_sq + EPSILON) * gain_heads)
        .astype(jnp.bfloat16)
        .reshape(rows, heads_here * HEAD_DIM)
    )
    width = residual.shape[1]
    full = width * groups
    weight_all = lax.all_gather(out_weight, "ctx", axis=0, tiled=True).reshape(
        groups, width, heads_here * HEAD_DIM
    )
    partial_proj = jnp.einsum(
        "tk,gck->gtc", normed, weight_all, preferred_element_type=jnp.float32
    ).astype(jnp.bfloat16)
    pieces = lax.all_to_all(partial_proj, "head", 0, 0, tiled=True)
    stream_mine = residual.astype(jnp.float32) + jnp.sum(pieces.astype(jnp.float32), axis=0)
    sq_part = jnp.sum(stream_mine * stream_mine, axis=1)
    sq_hi = sq_part.astype(jnp.bfloat16)
    sq_lo = (sq_part - sq_hi.astype(jnp.float32)).astype(jnp.bfloat16)
    extra = jnp.zeros((8, width), jnp.bfloat16)
    extra = extra.at[0].set(norm_gain)
    extra = extra.at[1, :rows].set(sq_hi)
    extra = extra.at[2, :rows].set(sq_lo)
    payload = jnp.concatenate([stream_mine.astype(jnp.bfloat16), extra], axis=0)
    gathered = lax.all_gather(payload, "head", axis=1, tiled=True)
    stream_wide = gathered[:rows].astype(jnp.float32)
    gain_full = gathered[rows].astype(jnp.float32)
    sq_parts = gathered[rows + 1 : rows + 3].astype(jnp.float32).reshape(2, groups, width)
    stream_sq = jnp.sum(sq_parts[:, :, :rows], axis=(0, 1))[:, None] / full
    moe_in = (stream_wide * lax.rsqrt(stream_sq + EPSILON) * gain_full).astype(jnp.bfloat16)
    experts = router.shape[1]
    capacity = 3 * rows * TOP // (2 * experts)
    logits = jnp.dot(moe_in, router, preferred_element_type=jnp.float32)
    picked_mask = expert_ids[:, :, None] == jnp.arange(experts, dtype=jnp.int32)[None, None, :]
    picked = jnp.sum(jnp.where(picked_mask, logits[:, None, :], 0.0), axis=-1)
    mix_weights = jax.nn.sigmoid(picked - picked[:, ::-1])
    flat_ids = expert_ids.reshape(-1)
    onehot = (flat_ids[:, None] == jnp.arange(experts, dtype=jnp.int32)[None, :]).astype(jnp.int32)
    before = jnp.cumsum(onehot, axis=0) - onehot
    position = jnp.sum(before * onehot, axis=1)
    slot = flat_ids * capacity + position
    owner = jnp.arange(rows * TOP, dtype=jnp.int32) // TOP
    slot_token = jnp.zeros((experts * capacity,), jnp.int32).at[slot].set(owner)
    filled = jnp.zeros((experts * capacity,), jnp.bool_).at[slot].set(True)
    blank = jnp.zeros((), jnp.bfloat16)
    outgoing = jnp.where(filled[:, None], moe_in[slot_token], blank).reshape(
        experts, capacity, full
    )
    arriving = lax.all_to_all(outgoing, "ctx", split_axis=0, concat_axis=0, tiled=True)
    flat = arriving.reshape(-1, full)
    gate = jnp.dot(flat, gate_weight[0], preferred_element_type=jnp.float32)
    up = jnp.dot(flat, up_weight[0], preferred_element_type=jnp.float32)
    activated = (jax.nn.silu(gate) * up).astype(jnp.bfloat16)
    down = down_weight[0].reshape(down_weight.shape[1], groups, width)
    partial_value = jnp.einsum(
        "rf,fgc->grc", activated, down, preferred_element_type=jnp.float32
    ).astype(jnp.bfloat16)
    summed = lax.psum_scatter(partial_value, "head", scatter_dimension=0, tiled=True)
    summed = summed.reshape(arriving.shape[0], arriving.shape[1], width)
    returned = lax.all_to_all(summed, "ctx", split_axis=0, concat_axis=0, tiled=True)
    picked_rows = returned.reshape(experts * capacity, width)[slot].astype(jnp.float32)
    moe_out = jnp.sum(picked_rows.reshape(rows, TOP, width) * mix_weights[:, :, None], axis=1)
    return stream_mine + moe_out


def solution(mesh):
    placed = (
        P("ctx", "head"),
        P("ctx", "head"),
        P("ctx", "head"),
        P("ctx", "head"),
        P("head"),
        P("ctx", "head"),
        P("ctx", "head"),
        P("head"),
        P(),
        P("ctx", None),
        P("ctx", None, "head"),
        P("ctx", None, "head"),
        P("ctx", "head", None),
    )
    return jax.shard_map(
        on_device, mesh=mesh, in_specs=placed, out_specs=P("ctx", "head"), check_vma=False
    )
```

```python
import jax
import jax.numpy as jnp
from jax import lax
from jax.sharding import PartitionSpec as P

HEAD_DIM = 128
TOP = 2


HIGH = lax.Precision.HIGHEST
EPSILON = 1e-05


def combine(earlier, later):
    rows = HEAD_DIM
    decay_late = later[:, rows:rows + 1, 0:1]
    state = decay_late * earlier[:, :rows] + later[:, :rows]
    decay = earlier[:, rows:rows + 1] * later[:, rows:rows + 1]
    pad = jnp.zeros((later.shape[0], later.shape[1] - rows - 1, later.shape[2]), later.dtype)
    return jnp.concatenate([state, decay, pad], axis=1)


def exclusive_scan(packed, axis):
    count, mine = lax.axis_size(axis), lax.axis_index(axis)
    rows = HEAD_DIM
    identity = jnp.zeros_like(packed).at[:, rows].set(1.0)
    window = packed
    before = identity
    base = 1
    while base < count:
        joined = None
        for step in range(1, 4):
            shift = step * base
            if shift >= count:
                break
            pairs = [(j, j + shift) for j in range(count - shift)]
            got = lax.ppermute(window, axis, pairs)
            got = jnp.where(mine >= shift, got, identity)
            joined = got if joined is None else combine(got, joined)
        before = combine(joined, before)
        if 4 * base < count:
            window = combine(joined, window)
        base *= 4
    return before[:, :rows]


def on_device(
    queries,
    key_rows,
    values,
    log_decay,
    head_gain,
    out_weight,
    residual,
    norm_gain,
    router,
    expert_ids,
    gate_weight,
    up_weight,
    down_weight,
):
    rows = queries.shape[0]
    heads_here = log_decay.shape[1]
    groups = lax.axis_size("head")
    query_heads = queries.reshape(rows, heads_here, HEAD_DIM)
    key_heads = key_rows.reshape(rows, heads_here, HEAD_DIM)
    value_heads = values.reshape(rows, heads_here, HEAD_DIM)
    cumulative = jnp.cumsum(log_decay, axis=0)
    scores = jnp.einsum("thd,jhd->htj", query_heads, key_heads, preferred_element_type=jnp.float32)
    causal = jnp.arange(rows)[:, None] >= jnp.arange(rows)[None, :]
    gap = cumulative.T[:, :, None] - cumulative.T[:, None, :]
    weight = jnp.where(causal[None], jnp.exp(-jnp.where(causal[None], gap, 0.0)), 0.0)
    weighted = (scores * weight).astype(jnp.bfloat16)
    inner = jnp.einsum("htj,jhd->thd", weighted, value_heads, preferred_element_type=jnp.float32)
    value_wide = value_heads.astype(jnp.float32)
    tail = jnp.exp(cumulative - cumulative[-1:])
    keys_tail = key_heads.astype(jnp.float32) * tail[:, :, None]
    local_state = jnp.einsum("jhd,jhe->hde", keys_tail, value_wide, precision=HIGH)
    shard_decay = jnp.exp(-cumulative[-1])
    decay_rows = jnp.broadcast_to(shard_decay[:, None, None], (heads_here, 1, HEAD_DIM))
    pad = jnp.zeros((heads_here, 7, HEAD_DIM), jnp.float32)
    packed = jnp.concatenate([local_state, decay_rows, pad], axis=1)
    incoming = exclusive_scan(packed, "ctx")
    query_decayed = query_heads.astype(jnp.float32) * jnp.exp(-cumulative)[:, :, None]
    outer = jnp.einsum("thd,hde->the", query_decayed, incoming, precision=HIGH)
    mixed = inner + outer
    mean_sq = jnp.mean(mixed * mixed, axis=-1, keepdims=True)
    gain_heads = head_gain.astype(jnp.float32).reshape(heads_here, HEAD_DIM)
    normed = (
        (mixed * lax.rsqrt(mean_sq + EPSILON) * gain_heads)
        .astype(jnp.bfloat16)
        .reshape(rows, heads_here * HEAD_DIM)
    )
    width = residual.shape[1]
    full = width * groups
    weight_all = lax.all_gather(out_weight, "ctx", axis=0, tiled=True).reshape(
        groups, width, heads_here * HEAD_DIM
    )
    partial_proj = jnp.einsum(
        "tk,gck->gtc", normed, weight_all, preferred_element_type=jnp.float32
    )
    total = lax.psum_scatter(partial_proj, "head", scatter_dimension=0, tiled=True)
    stream_mine = residual.astype(jnp.float32) + total[0]
    sq_part = jnp.sum(stream_mine * stream_mine, axis=1)
    sq_hi = sq_part.astype(jnp.bfloat16)
    sq_lo = (sq_part - sq_hi.astype(jnp.float32)).astype(jnp.bfloat16)
    extra = jnp.zeros((8, width), jnp.bfloat16)
    extra = extra.at[0].set(norm_gain)
    extra = extra.at[1, :rows].set(sq_hi)
    extra = extra.at[2, :rows].set(sq_lo)
    payload = jnp.concatenate([stream_mine.astype(jnp.bfloat16), extra], axis=0)
    gathered = lax.all_gather(payload, "head", axis=1, tiled=True)
    stream_wide = gathered[:rows].astype(jnp.float32)
    gain_full = gathered[rows].astype(jnp.float32)
    sq_parts = gathered[rows + 1 : rows + 3].astype(jnp.float32).reshape(2, groups, width)
    stream_sq = jnp.sum(sq_parts[:, :, :rows], axis=(0, 1))[:, None] / full
    moe_in = (stream_wide * lax.rsqrt(stream_sq + EPSILON) * gain_full).astype(jnp.bfloat16)
    experts = router.shape[1]
    capacity = 3 * rows * TOP // (2 * experts)
    logits = jnp.dot(moe_in, router, preferred_element_type=jnp.float32)
    picked_mask = expert_ids[:, :, None] == jnp.arange(experts, dtype=jnp.int32)[None, None, :]
    picked = jnp.sum(jnp.where(picked_mask, logits[:, None, :], 0.0), axis=-1)
    mix_weights = jax.nn.sigmoid(picked - picked[:, ::-1])
    flat_ids = expert_ids.reshape(-1)
    onehot = (flat_ids[:, None] == jnp.arange(experts, dtype=jnp.int32)[None, :]).astype(jnp.int32)
    before = jnp.cumsum(onehot, axis=0) - onehot
    position = jnp.sum(before * onehot, axis=1)
    slot = flat_ids * capacity + position
    owner = jnp.arange(rows * TOP, dtype=jnp.int32) // TOP
    slot_token = jnp.zeros((experts * capacity,), jnp.int32).at[slot].set(owner)
    filled = jnp.zeros((experts * capacity,), jnp.bool_).at[slot].set(True)
    blank = jnp.zeros((), jnp.bfloat16)
    outgoing = jnp.where(filled[:, None], moe_in[slot_token], blank).reshape(
        experts, capacity, full
    )
    half = capacity // 2
    down = down_weight[0].reshape(down_weight.shape[1], groups, width)
    parts = []
    for lo, hi in ((0, half), (half, capacity)):
        arriving = lax.all_to_all(outgoing[:, lo:hi], "ctx", split_axis=0, concat_axis=0, tiled=True)
        flat = arriving.reshape(-1, full)
        gate = jnp.dot(flat, gate_weight[0], preferred_element_type=jnp.float32)
        up = jnp.dot(flat, up_weight[0], preferred_element_type=jnp.float32)
        activated = (jax.nn.silu(gate) * up).astype(jnp.bfloat16)
        partial_value = jnp.einsum(
            "rf,fgc->grc", activated, down, preferred_element_type=jnp.float32
        ).astype(jnp.bfloat16)
        summed = lax.psum_scatter(partial_value, "head", scatter_dimension=0, tiled=True)
        summed = summed.reshape(arriving.shape[0], arriving.shape[1], width)
        parts.append(lax.all_to_all(summed, "ctx", split_axis=0, concat_axis=0, tiled=True))
    returned = jnp.concatenate(parts, axis=1)
    picked_rows = returned.reshape(experts * capacity, width)[slot].astype(jnp.float32)
    moe_out = jnp.sum(picked_rows.reshape(rows, TOP, width) * mix_weights[:, :, None], axis=1)
    return stream_mine + moe_out


def solution(mesh):
    placed = (
        P("ctx", "head"),
        P("ctx", "head"),
        P("ctx", "head"),
        P("ctx", "head"),
        P("head"),
        P("ctx", "head"),
        P("ctx", "head"),
        P("head"),
        P(),
        P("ctx", None),
        P("ctx", None, "head"),
        P("ctx", None, "head"),
        P("ctx", "head", None),
    )
    return jax.shard_map(
        on_device, mesh=mesh, in_specs=placed, out_specs=P("ctx", "head"), check_vma=False
    )
```

```python
import jax
import jax.numpy as jnp
from jax import lax
from jax.sharding import PartitionSpec as P

HEAD_DIM = 128
TOP = 2


HIGH = lax.Precision.HIGHEST
EPSILON = 1e-05


def combine(earlier, later):
    rows = HEAD_DIM
    decay_late = later[:, rows:rows + 1, 0:1]
    state = decay_late * earlier[:, :rows] + later[:, :rows]
    decay = earlier[:, rows:rows + 1] * later[:, rows:rows + 1]
    pad = jnp.zeros((later.shape[0], later.shape[1] - rows - 1, later.shape[2]), later.dtype)
    return jnp.concatenate([state, decay, pad], axis=1)


def exclusive_scan(packed, axis):
    count, mine = lax.axis_size(axis), lax.axis_index(axis)
    rows = HEAD_DIM
    identity = jnp.zeros_like(packed).at[:, rows].set(1.0)
    window = packed
    before = identity
    shift = 1
    while shift < count:
        pairs = [(j, j + shift) for j in range(count - shift)]
        got = lax.ppermute(window, axis, pairs)
        got = jnp.where(mine >= shift, got, identity)
        before = combine(got, before)
        if 2 * shift < count:
            window = combine(got, window)
        shift *= 2
    return before[:, :rows]


def on_device(
    queries,
    key_rows,
    values,
    log_decay,
    head_gain,
    out_weight,
    residual,
    norm_gain,
    router,
    expert_ids,
    gate_weight,
    up_weight,
    down_weight,
):
    rows = queries.shape[0]
    heads_here = log_decay.shape[1]
    groups = lax.axis_size("head")
    query_heads = queries.reshape(rows, heads_here, HEAD_DIM)
    key_heads = key_rows.reshape(rows, heads_here, HEAD_DIM)
    value_heads = values.reshape(rows, heads_here, HEAD_DIM)
    cumulative = jnp.cumsum(log_decay, axis=0)
    scores = jnp.einsum("thd,jhd->htj", query_heads, key_heads, preferred_element_type=jnp.float32)
    causal = jnp.arange(rows)[:, None] >= jnp.arange(rows)[None, :]
    gap = cumulative.T[:, :, None] - cumulative.T[:, None, :]
    weight = jnp.where(causal[None], jnp.exp(-jnp.where(causal[None], gap, 0.0)), 0.0)
    weighted = (scores * weight).astype(jnp.bfloat16)
    inner = jnp.einsum("htj,jhd->thd", weighted, value_heads, preferred_element_type=jnp.float32)
    value_wide = value_heads.astype(jnp.float32)
    tail = jnp.exp(cumulative - cumulative[-1:])
    keys_tail = key_heads.astype(jnp.float32) * tail[:, :, None]
    local_state = jnp.einsum("jhd,jhe->hde", keys_tail, value_wide, precision=HIGH)
    shard_decay = jnp.exp(-cumulative[-1])
    decay_rows = jnp.broadcast_to(shard_decay[:, None, None], (heads_here, 1, HEAD_DIM))
    pad = jnp.zeros((heads_here, 7, HEAD_DIM), jnp.float32)
    packed = jnp.concatenate([local_state, decay_rows, pad], axis=1)
    incoming = exclusive_scan(packed, "ctx")
    query_decayed = query_heads.astype(jnp.float32) * jnp.exp(-cumulative)[:, :, None]
    outer = jnp.einsum("thd,hde->the", query_decayed, incoming, precision=HIGH)
    mixed = inner + outer
    mean_sq = jnp.mean(mixed * mixed, axis=-1, keepdims=True)
    gain_heads = head_gain.astype(jnp.float32).reshape(heads_here, HEAD_DIM)
    normed = (
        (mixed * lax.rsqrt(mean_sq + EPSILON) * gain_heads)
        .astype(jnp.bfloat16)
        .reshape(rows, heads_here * HEAD_DIM)
    )
    width = residual.shape[1]
    full = width * groups
    weight_all = lax.all_gather(out_weight, "ctx", axis=0, tiled=True).reshape(
        groups, width, heads_here * HEAD_DIM
    )
    partial_proj = jnp.einsum(
        "tk,gck->gtc", normed, weight_all, preferred_element_type=jnp.float32
    ).astype(jnp.bfloat16)
    total = lax.psum_scatter(partial_proj, "head", scatter_dimension=0, tiled=True)
    stream_mine = residual.astype(jnp.float32) + total[0].astype(jnp.float32)
    sq_part = jnp.sum(stream_mine * stream_mine, axis=1)
    sq_hi = sq_part.astype(jnp.bfloat16)
    sq_lo = (sq_part - sq_hi.astype(jnp.float32)).astype(jnp.bfloat16)
    extra = jnp.zeros((8, width), jnp.bfloat16)
    extra = extra.at[0].set(norm_gain)
    extra = extra.at[1, :rows].set(sq_hi)
    extra = extra.at[2, :rows].set(sq_lo)
    payload = jnp.concatenate([stream_mine.astype(jnp.bfloat16), extra], axis=0)
    gathered = lax.all_gather(payload, "head", axis=1, tiled=True)
    stream_wide = gathered[:rows].astype(jnp.float32)
    gain_full = gathered[rows].astype(jnp.float32)
    sq_parts = gathered[rows + 1 : rows + 3].astype(jnp.float32).reshape(2, groups, width)
    stream_sq = jnp.sum(sq_parts[:, :, :rows], axis=(0, 1))[:, None] / full
    moe_in = (stream_wide * lax.rsqrt(stream_sq + EPSILON) * gain_full).astype(jnp.bfloat16)
    experts = router.shape[1]
    capacity = 3 * rows * TOP // (2 * experts)
    logits = jnp.dot(moe_in, router, preferred_element_type=jnp.float32)
    picked_mask = expert_ids[:, :, None] == jnp.arange(experts, dtype=jnp.int32)[None, None, :]
    picked = jnp.sum(jnp.where(picked_mask, logits[:, None, :], 0.0), axis=-1)
    mix_weights = jax.nn.sigmoid(picked - picked[:, ::-1])
    flat_ids = expert_ids.reshape(-1)
    onehot = (flat_ids[:, None] == jnp.arange(experts, dtype=jnp.int32)[None, :]).astype(jnp.int32)
    before = jnp.cumsum(onehot, axis=0) - onehot
    position = jnp.sum(before * onehot, axis=1)
    slot = flat_ids * capacity + position
    owner = jnp.arange(rows * TOP, dtype=jnp.int32) // TOP
    slot_token = jnp.full((experts * capacity,), rows, jnp.int32).at[slot].set(owner)
    padded = jnp.concatenate([moe_in, jnp.zeros((8, full), jnp.bfloat16)], axis=0)
    outgoing = padded[slot_token].reshape(experts, capacity, full)
    arriving = lax.all_to_all(outgoing, "ctx", split_axis=0, concat_axis=0, tiled=True)
    flat = arriving.reshape(-1, full)
    gate = jnp.dot(flat, gate_weight[0], preferred_element_type=jnp.float32)
    up = jnp.dot(flat, up_weight[0], preferred_element_type=jnp.float32)
    activated = (jax.nn.silu(gate) * up).astype(jnp.bfloat16)
    down = down_weight[0].reshape(down_weight.shape[1], groups, width)
    partial_value = jnp.einsum(
        "rf,fgc->grc", activated, down, preferred_element_type=jnp.float32
    ).astype(jnp.bfloat16)
    summed = lax.psum_scatter(partial_value, "head", scatter_dimension=0, tiled=True)
    summed = summed.reshape(arriving.shape[0], arriving.shape[1], width)
    returned = lax.all_to_all(summed, "ctx", split_axis=0, concat_axis=0, tiled=True)
    picked_rows = returned.reshape(experts * capacity, width)[slot].astype(jnp.float32)
    moe_out = jnp.sum(picked_rows.reshape(rows, TOP, width) * mix_weights[:, :, None], axis=1)
    return stream_mine + moe_out


def solution(mesh):
    placed = (
        P("ctx", "head"),
        P("ctx", "head"),
        P("ctx", "head"),
        P("ctx", "head"),
        P("head"),
        P("ctx", "head"),
        P("ctx", "head"),
        P("head"),
        P(),
        P("ctx", None),
        P("ctx", None, "head"),
        P("ctx", None, "head"),
        P("ctx", "head", None),
    )
    return jax.shard_map(
        on_device, mesh=mesh, in_specs=placed, out_specs=P("ctx", "head"), check_vma=False
    )
```

```python
import jax
import jax.numpy as jnp
from jax import lax
from jax.sharding import PartitionSpec as P

HEAD_DIM = 128
TOP = 2


HIGH = lax.Precision.HIGHEST
EPSILON = 1e-05


def combine(earlier, later):
    rows = HEAD_DIM
    decay_late = later[:, rows:rows + 1, 0:1]
    state = decay_late * earlier[:, :rows] + later[:, :rows]
    decay = earlier[:, rows:rows + 1] * later[:, rows:rows + 1]
    pad = jnp.zeros((later.shape[0], later.shape[1] - rows - 1, later.shape[2]), later.dtype)
    return jnp.concatenate([state, decay, pad], axis=1)


def exclusive_scan(packed, axis):
    count, mine = lax.axis_size(axis), lax.axis_index(axis)
    rows = HEAD_DIM
    identity = jnp.zeros_like(packed).at[:, rows].set(1.0)
    window = packed
    before = identity
    shift = 1
    while shift < count:
        pairs = [(j, j + shift) for j in range(count - shift)]
        got = lax.ppermute(window, axis, pairs)
        got = jnp.where(mine >= shift, got, identity)
        before = combine(got, before)
        if 2 * shift < count:
            window = combine(got, window)
        shift *= 2
    return before[:, :rows]


def on_device(
    queries,
    key_rows,
    values,
    log_decay,
    head_gain,
    out_weight,
    residual,
    norm_gain,
    router,
    expert_ids,
    gate_weight,
    up_weight,
    down_weight,
):
    rows = queries.shape[0]
    heads_here = log_decay.shape[1]
    groups = lax.axis_size("head")
    query_heads = queries.reshape(rows, heads_here, HEAD_DIM)
    key_heads = key_rows.reshape(rows, heads_here, HEAD_DIM)
    value_heads = values.reshape(rows, heads_here, HEAD_DIM)
    cumulative = jnp.cumsum(log_decay, axis=0)
    scores = jnp.einsum("thd,jhd->htj", query_heads, key_heads, preferred_element_type=jnp.float32)
    causal = jnp.arange(rows)[:, None] >= jnp.arange(rows)[None, :]
    gap = cumulative.T[:, :, None] - cumulative.T[:, None, :]
    weight = jnp.where(causal[None], jnp.exp(-jnp.where(causal[None], gap, 0.0)), 0.0)
    weighted = (scores * weight).astype(jnp.bfloat16)
    inner = jnp.einsum("htj,jhd->thd", weighted, value_heads, preferred_element_type=jnp.float32)
    value_wide = value_heads.astype(jnp.float32)
    tail = jnp.exp(cumulative - cumulative[-1:])
    keys_tail = key_heads.astype(jnp.float32) * tail[:, :, None]
    local_state = jnp.einsum("jhd,jhe->hde", keys_tail, value_wide, precision=HIGH)
    shard_decay = jnp.exp(-cumulative[-1])
    decay_rows = jnp.broadcast_to(shard_decay[:, None, None], (heads_here, 1, HEAD_DIM))
    pad = jnp.zeros((heads_here, 7, HEAD_DIM), jnp.float32)
    packed = jnp.concatenate([local_state, decay_rows, pad], axis=1)
    incoming = exclusive_scan(packed, "ctx")
    query_decayed = query_heads.astype(jnp.float32) * jnp.exp(-cumulative)[:, :, None]
    outer = jnp.einsum("thd,hde->the", query_decayed, incoming, precision=HIGH)
    mixed = inner + outer
    mean_sq = jnp.mean(mixed * mixed, axis=-1, keepdims=True)
    gain_heads = head_gain.astype(jnp.float32).reshape(heads_here, HEAD_DIM)
    normed = (
        (mixed * lax.rsqrt(mean_sq + EPSILON) * gain_heads)
        .astype(jnp.bfloat16)
        .reshape(rows, heads_here * HEAD_DIM)
    )
    width = residual.shape[1]
    full = width * groups
    weight_all = lax.all_gather(out_weight, "ctx", axis=0, tiled=True)
    partial_proj = lax.dot_general(
        normed, weight_all, (((1,), (1,)), ((), ())), preferred_element_type=jnp.float32
    )
    mine = lax.axis_index("head")
    own = (jnp.arange(full) // width) == mine
    resid_wide = jnp.tile(residual.astype(jnp.float32), (1, groups))
    partial_proj = jnp.where(own[None, :], partial_proj + resid_wide, partial_proj)
    gain_wide = jnp.where(own, jnp.tile(norm_gain, groups), jnp.zeros((), jnp.bfloat16))
    extra = jnp.zeros((8, full), jnp.bfloat16).at[0].set(gain_wide)
    payload = jnp.concatenate([partial_proj.astype(jnp.bfloat16), extra], axis=0)
    summed_all = lax.psum(payload, "head")
    stream_wide = summed_all[:rows].astype(jnp.float32)
    gain_full = summed_all[rows].astype(jnp.float32)
    stream_sq = jnp.mean(stream_wide * stream_wide, axis=-1, keepdims=True)
    moe_in = (stream_wide * lax.rsqrt(stream_sq + EPSILON) * gain_full).astype(jnp.bfloat16)
    stream_mine = lax.dynamic_slice_in_dim(stream_wide, mine * width, width, 1)
    experts = router.shape[1]
    capacity = 3 * rows * TOP // (2 * experts)
    logits = jnp.dot(moe_in, router, preferred_element_type=jnp.float32)
    picked_mask = expert_ids[:, :, None] == jnp.arange(experts, dtype=jnp.int32)[None, None, :]
    picked = jnp.sum(jnp.where(picked_mask, logits[:, None, :], 0.0), axis=-1)
    mix_weights = jax.nn.sigmoid(picked - picked[:, ::-1])
    flat_ids = expert_ids.reshape(-1)
    onehot = (flat_ids[:, None] == jnp.arange(experts, dtype=jnp.int32)[None, :]).astype(jnp.int32)
    before = jnp.cumsum(onehot, axis=0) - onehot
    position = jnp.sum(before * onehot, axis=1)
    slot = flat_ids * capacity + position
    owner = jnp.arange(rows * TOP, dtype=jnp.int32) // TOP
    slot_token = jnp.full((experts * capacity,), rows, jnp.int32).at[slot].set(owner)
    padded = jnp.concatenate([moe_in, jnp.zeros((8, full), jnp.bfloat16)], axis=0)
    outgoing = padded[slot_token].reshape(experts, capacity, full)
    arriving = lax.all_to_all(outgoing, "ctx", split_axis=0, concat_axis=0, tiled=True)
    flat = arriving.reshape(-1, full)
    gate = jnp.dot(flat, gate_weight[0], preferred_element_type=jnp.float32)
    up = jnp.dot(flat, up_weight[0], preferred_element_type=jnp.float32)
    activated = (jax.nn.silu(gate) * up).astype(jnp.bfloat16)
    down = down_weight[0].reshape(down_weight.shape[1], groups, width)
    partial_value = jnp.einsum(
        "rf,fgc->grc", activated, down, preferred_element_type=jnp.float32
    ).astype(jnp.bfloat16)
    summed = lax.psum_scatter(partial_value, "head", scatter_dimension=0, tiled=True)
    summed = summed.reshape(arriving.shape[0], arriving.shape[1], width)
    returned = lax.all_to_all(summed, "ctx", split_axis=0, concat_axis=0, tiled=True)
    picked_rows = returned.reshape(experts * capacity, width)[slot].astype(jnp.float32)
    moe_out = jnp.sum(picked_rows.reshape(rows, TOP, width) * mix_weights[:, :, None], axis=1)
    return stream_mine + moe_out


def solution(mesh):
    placed = (
        P("ctx", "head"),
        P("ctx", "head"),
        P("ctx", "head"),
        P("ctx", "head"),
        P("head"),
        P("ctx", "head"),
        P("ctx", "head"),
        P("head"),
        P(),
        P("ctx", None),
        P("ctx", None, "head"),
        P("ctx", None, "head"),
        P("ctx", "head", None),
    )
    return jax.shard_map(
        on_device, mesh=mesh, in_specs=placed, out_specs=P("ctx", "head"), check_vma=False
    )
```

```python
import jax
import jax.numpy as jnp
from jax import lax
from jax.sharding import PartitionSpec as P

HEAD_DIM = 128
TOP = 2


HIGH = lax.Precision.HIGHEST
EPSILON = 1e-05


def combine(earlier, later):
    rows = HEAD_DIM
    decay_late = later[:, rows:rows + 1, 0:1]
    state = decay_late * earlier[:, :rows] + later[:, :rows]
    decay = earlier[:, rows:rows + 1] * later[:, rows:rows + 1]
    pad = jnp.zeros((later.shape[0], later.shape[1] - rows - 1, later.shape[2]), later.dtype)
    return jnp.concatenate([state, decay, pad], axis=1)


def exclusive_scan(packed, axis):
    count, mine = lax.axis_size(axis), lax.axis_index(axis)
    rows = HEAD_DIM
    identity = jnp.zeros_like(packed).at[:, rows].set(1.0)
    window = packed
    before = identity
    shift = 1
    while shift < count:
        pairs = [(j, j + shift) for j in range(count - shift)]
        got = lax.ppermute(window, axis, pairs)
        got = jnp.where(mine >= shift, got, identity)
        before = combine(got, before)
        if 2 * shift < count:
            window = combine(got, window)
        shift *= 2
    return before[:, :rows]


def on_device(
    queries,
    key_rows,
    values,
    log_decay,
    head_gain,
    out_weight,
    residual,
    norm_gain,
    router,
    expert_ids,
    gate_weight,
    up_weight,
    down_weight,
):
    rows = queries.shape[0]
    heads_here = log_decay.shape[1]
    groups = lax.axis_size("head")
    query_heads = queries.reshape(rows, heads_here, HEAD_DIM)
    key_heads = key_rows.reshape(rows, heads_here, HEAD_DIM)
    value_heads = values.reshape(rows, heads_here, HEAD_DIM)
    cumulative = jnp.cumsum(log_decay, axis=0)
    scores = jnp.einsum("thd,jhd->htj", query_heads, key_heads, preferred_element_type=jnp.float32)
    causal = jnp.arange(rows)[:, None] >= jnp.arange(rows)[None, :]
    gap = cumulative.T[:, :, None] - cumulative.T[:, None, :]
    weight = jnp.where(causal[None], jnp.exp(-jnp.where(causal[None], gap, 0.0)), 0.0)
    weighted = (scores * weight).astype(jnp.bfloat16)
    inner = jnp.einsum("htj,jhd->thd", weighted, value_heads, preferred_element_type=jnp.float32)
    value_wide = value_heads.astype(jnp.float32)
    tail = jnp.exp(cumulative - cumulative[-1:])
    keys_tail = key_heads.astype(jnp.float32) * tail[:, :, None]
    local_state = jnp.einsum("jhd,jhe->hde", keys_tail, value_wide, precision=HIGH)
    shard_decay = jnp.exp(-cumulative[-1])
    decay_rows = jnp.broadcast_to(shard_decay[:, None, None], (heads_here, 1, HEAD_DIM))
    pad = jnp.zeros((heads_here, 7, HEAD_DIM), jnp.float32)
    packed = jnp.concatenate([local_state, decay_rows, pad], axis=1)
    incoming = exclusive_scan(packed, "ctx")
    query_decayed = query_heads.astype(jnp.float32) * jnp.exp(-cumulative)[:, :, None]
    outer = jnp.einsum("thd,hde->the", query_decayed, incoming, precision=HIGH)
    mixed = inner + outer
    mean_sq = jnp.mean(mixed * mixed, axis=-1, keepdims=True)
    gain_heads = head_gain.astype(jnp.float32).reshape(heads_here, HEAD_DIM)
    normed = (
        (mixed * lax.rsqrt(mean_sq + EPSILON) * gain_heads)
        .astype(jnp.bfloat16)
        .reshape(rows, heads_here * HEAD_DIM)
    )
    width = residual.shape[1]
    full = width * groups
    weight_all = lax.all_gather(out_weight, "ctx", axis=0, tiled=True).reshape(
        groups, width, heads_here * HEAD_DIM
    )
    partial_proj = jnp.einsum(
        "tk,gck->gtc", normed, weight_all, preferred_element_type=jnp.float32
    ).astype(jnp.bfloat16)
    total = lax.psum_scatter(partial_proj, "head", scatter_dimension=0, tiled=True)
    stream_mine = residual.astype(jnp.float32) + total[0].astype(jnp.float32)
    sq_part = jnp.sum(stream_mine * stream_mine, axis=1)
    sq_hi = sq_part.astype(jnp.bfloat16)
    sq_lo = (sq_part - sq_hi.astype(jnp.float32)).astype(jnp.bfloat16)
    experts = router.shape[1]
    capacity = 3 * rows * TOP // (2 * experts)
    lane = 128
    wide = width + lane
    other_id = expert_ids[:, ::-1].astype(jnp.bfloat16)
    token_rows = jnp.concatenate(
        [
            stream_mine.astype(jnp.bfloat16),
            sq_hi[:, None],
            sq_lo[:, None],
            jnp.zeros((rows, lane - 2), jnp.bfloat16),
        ],
        axis=1,
    )
    token_rows = jnp.concatenate([token_rows, jnp.zeros((8, wide), jnp.bfloat16)], axis=0)
    flat_ids = expert_ids.reshape(-1)
    onehot = (flat_ids[:, None] == jnp.arange(experts, dtype=jnp.int32)[None, :]).astype(jnp.int32)
    before = jnp.cumsum(onehot, axis=0) - onehot
    position = jnp.sum(before * onehot, axis=1)
    slot = flat_ids * capacity + position
    owner = jnp.arange(rows * TOP, dtype=jnp.int32) // TOP
    slot_token = jnp.full((experts * capacity,), rows, jnp.int32).at[slot].set(owner)
    slot_other = jnp.zeros((experts * capacity,), jnp.bfloat16).at[slot].set(other_id.reshape(-1))
    outgoing = token_rows[slot_token]
    outgoing = outgoing.at[:, width + 2].set(slot_other).reshape(experts, capacity, wide)
    arriving = lax.all_to_all(outgoing, "ctx", split_axis=0, concat_axis=0, tiled=True)
    flat = arriving.reshape(-1, wide)
    gain_row = jnp.concatenate([norm_gain, jnp.zeros((lane,), jnp.bfloat16)])
    gain_rows = jnp.zeros((8, wide), jnp.bfloat16).at[0].set(gain_row)
    gathered = lax.all_gather(jnp.concatenate([flat, gain_rows], axis=0), "head", axis=1, tiled=True)
    slots_here = flat.shape[0]
    blocks = gathered.reshape(slots_here + 8, groups, wide)
    stream_wide = blocks[:slots_here, :, :width].reshape(slots_here, full).astype(jnp.float32)
    gain_full = blocks[slots_here, :, :width].reshape(full).astype(jnp.float32)
    sq_parts = blocks[:slots_here, :, width:width + 2].astype(jnp.float32)
    stream_sq = jnp.sum(sq_parts, axis=(1, 2))[:, None] / full
    other_here = blocks[:slots_here, 0, width + 2].astype(jnp.int32)
    moe_in = (stream_wide * lax.rsqrt(stream_sq + EPSILON) * gain_full).astype(jnp.bfloat16)
    logits = jnp.dot(moe_in, router, preferred_element_type=jnp.float32)
    expert_here = lax.axis_index("ctx")
    names = jnp.arange(experts, dtype=jnp.int32)[None, :]
    own_logit = jnp.sum(jnp.where(names == expert_here, logits, 0.0), axis=1)
    other_logit = jnp.sum(jnp.where(names == other_here[:, None], logits, 0.0), axis=1)
    mix_here = jax.nn.sigmoid(own_logit - other_logit)
    mix_hi = mix_here.astype(jnp.bfloat16)
    mix_lo = (mix_here - mix_hi.astype(jnp.float32)).astype(jnp.bfloat16)
    gate = jnp.dot(moe_in, gate_weight[0], preferred_element_type=jnp.float32)
    up = jnp.dot(moe_in, up_weight[0], preferred_element_type=jnp.float32)
    activated = (jax.nn.silu(gate) * up).astype(jnp.bfloat16)
    down = down_weight[0].reshape(down_weight.shape[1], groups, width)
    partial_value = jnp.einsum(
        "rf,fgc->grc", activated, down, preferred_element_type=jnp.float32
    ).astype(jnp.bfloat16)
    summed = lax.psum_scatter(partial_value, "head", scatter_dimension=0, tiled=True)[0]
    back = jnp.concatenate(
        [
            summed,
            mix_hi[:, None],
            mix_lo[:, None],
            jnp.zeros((slots_here, lane - 2), jnp.bfloat16),
        ],
        axis=1,
    ).reshape(arriving.shape[0], arriving.shape[1], wide)
    returned = lax.all_to_all(back, "ctx", split_axis=0, concat_axis=0, tiled=True)
    picked_rows = returned.reshape(experts * capacity, wide)[slot].astype(jnp.float32)
    picked_rows = picked_rows.reshape(rows, TOP, wide)
    mix_weights = picked_rows[:, :, width] + picked_rows[:, :, width + 1]
    moe_out = jnp.sum(picked_rows[:, :, :width] * mix_weights[:, :, None], axis=1)
    return stream_mine + moe_out


def solution(mesh):
    placed = (
        P("ctx", "head"),
        P("ctx", "head"),
        P("ctx", "head"),
        P("ctx", "head"),
        P("head"),
        P("ctx", "head"),
        P("ctx", "head"),
        P("head"),
        P(),
        P("ctx", None),
        P("ctx", None, "head"),
        P("ctx", None, "head"),
        P("ctx", "head", None),
    )
    return jax.shard_map(
        on_device, mesh=mesh, in_specs=placed, out_specs=P("ctx", "head"), check_vma=False
    )
```

```python
import jax
import jax.numpy as jnp
from jax import lax
from jax.sharding import PartitionSpec as P

HEAD_DIM = 128
TOP = 2


HIGH = lax.Precision.HIGHEST
EPSILON = 1e-05


def combine(earlier, later):
    rows = HEAD_DIM
    decay_late = later[:, rows:rows + 1, 0:1]
    state = decay_late * earlier[:, :rows] + later[:, :rows]
    decay = earlier[:, rows:rows + 1] * later[:, rows:rows + 1]
    pad = jnp.zeros((later.shape[0], later.shape[1] - rows - 1, later.shape[2]), later.dtype)
    return jnp.concatenate([state, decay, pad], axis=1)


def exclusive_scan(packed, axis):
    count, mine = lax.axis_size(axis), lax.axis_index(axis)
    rows = HEAD_DIM
    identity = jnp.zeros_like(packed).at[:, rows].set(1.0)
    window = packed
    before = identity
    shift = 1
    while shift < count:
        pairs = [(j, j + shift) for j in range(count - shift)]
        got = lax.ppermute(window, axis, pairs)
        got = jnp.where(mine >= shift, got, identity)
        before = combine(got, before)
        if 2 * shift < count:
            window = combine(got, window)
        shift *= 2
    return before[:, :rows]


def on_device(
    queries,
    key_rows,
    values,
    log_decay,
    head_gain,
    out_weight,
    residual,
    norm_gain,
    router,
    expert_ids,
    gate_weight,
    up_weight,
    down_weight,
):
    rows = queries.shape[0]
    heads_here = log_decay.shape[1]
    groups = lax.axis_size("head")
    query_heads = queries.reshape(rows, heads_here, HEAD_DIM)
    key_heads = key_rows.reshape(rows, heads_here, HEAD_DIM)
    value_heads = values.reshape(rows, heads_here, HEAD_DIM)
    cumulative = jnp.cumsum(log_decay, axis=0)
    scores = jnp.einsum("thd,jhd->htj", query_heads, key_heads, preferred_element_type=jnp.float32)
    causal = jnp.arange(rows)[:, None] >= jnp.arange(rows)[None, :]
    gap = cumulative.T[:, :, None] - cumulative.T[:, None, :]
    weight = jnp.where(causal[None], jnp.exp(-jnp.where(causal[None], gap, 0.0)), 0.0)
    weighted = (scores * weight).astype(jnp.bfloat16)
    inner = jnp.einsum("htj,jhd->thd", weighted, value_heads, preferred_element_type=jnp.float32)
    value_wide = value_heads.astype(jnp.float32)
    tail = jnp.exp(cumulative - cumulative[-1:])
    keys_tail = key_heads.astype(jnp.float32) * tail[:, :, None]
    local_state = jnp.einsum("jhd,jhe->hde", keys_tail, value_wide, precision=HIGH)
    shard_decay = jnp.exp(-cumulative[-1])
    decay_rows = jnp.broadcast_to(shard_decay[:, None, None], (heads_here, 1, HEAD_DIM))
    pad = jnp.zeros((heads_here, 7, HEAD_DIM), jnp.float32)
    packed = jnp.concatenate([local_state, decay_rows, pad], axis=1)
    incoming = exclusive_scan(packed, "ctx")
    query_decayed = query_heads.astype(jnp.float32) * jnp.exp(-cumulative)[:, :, None]
    outer = jnp.einsum("thd,hde->the", query_decayed, incoming, precision=HIGH)
    mixed = inner + outer
    mean_sq = jnp.mean(mixed * mixed, axis=-1, keepdims=True)
    gain_heads = head_gain.astype(jnp.float32).reshape(heads_here, HEAD_DIM)
    normed = (
        (mixed * lax.rsqrt(mean_sq + EPSILON) * gain_heads)
        .astype(jnp.bfloat16)
        .reshape(rows, heads_here * HEAD_DIM)
    )
    width = residual.shape[1]
    full = width * groups
    weight_all = lax.all_gather(out_weight, "ctx", axis=0, tiled=True).reshape(
        groups, width, heads_here * HEAD_DIM
    )
    partial_proj = jnp.einsum(
        "tk,gck->gtc", normed, weight_all, preferred_element_type=jnp.float32
    ).astype(jnp.bfloat16)
    total = lax.psum_scatter(partial_proj, "head", scatter_dimension=0, tiled=True)
    stream_mine = residual.astype(jnp.float32) + total[0].astype(jnp.float32)
    sq_part = jnp.sum(stream_mine * stream_mine, axis=1)
    sq_hi = sq_part.astype(jnp.bfloat16)
    sq_lo = (sq_part - sq_hi.astype(jnp.float32)).astype(jnp.bfloat16)
    experts = router.shape[1]
    capacity = 3 * rows * TOP // (2 * experts)
    lane = 128
    wide = width + lane
    other_id = expert_ids[:, ::-1].astype(jnp.bfloat16)
    token_rows = jnp.concatenate(
        [
            stream_mine.astype(jnp.bfloat16),
            sq_hi[:, None],
            sq_lo[:, None],
            jnp.zeros((rows, lane - 2), jnp.bfloat16),
        ],
        axis=1,
    )
    token_rows = jnp.concatenate([token_rows, jnp.zeros((8, wide), jnp.bfloat16)], axis=0)
    flat_ids = expert_ids.reshape(-1)
    onehot = (flat_ids[:, None] == jnp.arange(experts, dtype=jnp.int32)[None, :]).astype(jnp.int32)
    before = jnp.cumsum(onehot, axis=0) - onehot
    position = jnp.sum(before * onehot, axis=1)
    slot = flat_ids * capacity + position
    owner = jnp.arange(rows * TOP, dtype=jnp.int32) // TOP
    slot_token = jnp.full((experts * capacity,), rows, jnp.int32).at[slot].set(owner)
    slot_other = jnp.zeros((experts * capacity,), jnp.bfloat16).at[slot].set(other_id.reshape(-1))
    outgoing = token_rows[slot_token]
    outgoing = outgoing.at[:, width + 2].set(slot_other).reshape(experts, capacity, wide)
    arriving = lax.all_to_all(outgoing, "ctx", split_axis=0, concat_axis=0, tiled=True)
    flat = arriving.reshape(-1, wide)
    gain_row = jnp.concatenate([norm_gain, jnp.zeros((lane,), jnp.bfloat16)])
    gain_rows = jnp.zeros((8, wide), jnp.bfloat16).at[0].set(gain_row)
    gathered = lax.all_gather(jnp.concatenate([flat, gain_rows], axis=0), "head", axis=0)
    slots_here = flat.shape[0]
    stream_blocks = gathered[:, :slots_here, :width].astype(jnp.float32)
    gain_blocks = gathered[:, slots_here, :width].astype(jnp.float32)
    sq_parts = gathered[:, :slots_here, width:width + 2].astype(jnp.float32)
    stream_sq = jnp.sum(sq_parts, axis=(0, 2))[None, :, None] / full
    other_here = flat[:, width + 2].astype(jnp.int32)
    moe_in = (stream_blocks * lax.rsqrt(stream_sq + EPSILON) * gain_blocks[:, None, :]).astype(
        jnp.bfloat16
    )
    router_blocks = router.reshape(groups, width, router.shape[1])
    logits = jnp.einsum("grc,gce->re", moe_in, router_blocks, preferred_element_type=jnp.float32)
    expert_here = lax.axis_index("ctx")
    names = jnp.arange(experts, dtype=jnp.int32)[None, :]
    own_logit = jnp.sum(jnp.where(names == expert_here, logits, 0.0), axis=1)
    other_logit = jnp.sum(jnp.where(names == other_here[:, None], logits, 0.0), axis=1)
    mix_here = jax.nn.sigmoid(own_logit - other_logit)
    mix_hi = mix_here.astype(jnp.bfloat16)
    mix_lo = (mix_here - mix_hi.astype(jnp.float32)).astype(jnp.bfloat16)
    hidden = gate_weight.shape[2]
    gate = jnp.einsum(
        "grc,gcf->rf", moe_in, gate_weight[0].reshape(groups, width, hidden),
        preferred_element_type=jnp.float32,
    )
    up = jnp.einsum(
        "grc,gcf->rf", moe_in, up_weight[0].reshape(groups, width, hidden),
        preferred_element_type=jnp.float32,
    )
    activated = (jax.nn.silu(gate) * up).astype(jnp.bfloat16)
    down = down_weight[0].reshape(down_weight.shape[1], groups, width)
    partial_value = jnp.einsum(
        "rf,fgc->grc", activated, down, preferred_element_type=jnp.float32
    ).astype(jnp.bfloat16)
    summed = lax.psum_scatter(partial_value, "head", scatter_dimension=0, tiled=True)[0]
    back = jnp.concatenate(
        [
            summed,
            mix_hi[:, None],
            mix_lo[:, None],
            jnp.zeros((slots_here, lane - 2), jnp.bfloat16),
        ],
        axis=1,
    ).reshape(arriving.shape[0], arriving.shape[1], wide)
    returned = lax.all_to_all(back, "ctx", split_axis=0, concat_axis=0, tiled=True)
    picked_rows = returned.reshape(experts * capacity, wide)[slot].astype(jnp.float32)
    picked_rows = picked_rows.reshape(rows, TOP, wide)
    mix_weights = picked_rows[:, :, width] + picked_rows[:, :, width + 1]
    moe_out = jnp.sum(picked_rows[:, :, :width] * mix_weights[:, :, None], axis=1)
    return stream_mine + moe_out


def solution(mesh):
    placed = (
        P("ctx", "head"),
        P("ctx", "head"),
        P("ctx", "head"),
        P("ctx", "head"),
        P("head"),
        P("ctx", "head"),
        P("ctx", "head"),
        P("head"),
        P(),
        P("ctx", None),
        P("ctx", None, "head"),
        P("ctx", None, "head"),
        P("ctx", "head", None),
    )
    return jax.shard_map(
        on_device, mesh=mesh, in_specs=placed, out_specs=P("ctx", "head"), check_vma=False
    )
```

```python
import jax
import jax.numpy as jnp
from jax import lax
from jax.sharding import PartitionSpec as P

HEAD_DIM = 128
TOP = 2


HIGH = lax.Precision.HIGHEST
EPSILON = 1e-05


def combine(earlier, later):
    rows = HEAD_DIM
    decay_late = later[:, rows:rows + 1, 0:1]
    state = decay_late * earlier[:, :rows] + later[:, :rows]
    decay = earlier[:, rows:rows + 1] * later[:, rows:rows + 1]
    pad = jnp.zeros((later.shape[0], later.shape[1] - rows - 1, later.shape[2]), later.dtype)
    return jnp.concatenate([state, decay, pad], axis=1)


def exclusive_scan(packed, axis):
    count, mine = lax.axis_size(axis), lax.axis_index(axis)
    rows = HEAD_DIM
    identity = jnp.zeros_like(packed).at[:, rows].set(1.0)
    window = packed
    before = identity
    shift = 1
    while shift < count:
        pairs = [(j, j + shift) for j in range(count - shift)]
        got = lax.ppermute(window, axis, pairs)
        got = jnp.where(mine >= shift, got, identity)
        before = combine(got, before)
        if 2 * shift < count:
            window = combine(got, window)
        shift *= 2
    return before[:, :rows]


def on_device(
    queries,
    key_rows,
    values,
    log_decay,
    head_gain,
    out_weight,
    residual,
    norm_gain,
    router,
    expert_ids,
    gate_weight,
    up_weight,
    down_weight,
):
    rows = queries.shape[0]
    heads_here = log_decay.shape[1]
    groups = lax.axis_size("head")
    query_heads = queries.reshape(rows, heads_here, HEAD_DIM)
    key_heads = key_rows.reshape(rows, heads_here, HEAD_DIM)
    value_heads = values.reshape(rows, heads_here, HEAD_DIM)
    cumulative = jnp.cumsum(log_decay, axis=0)
    scores = jnp.einsum("thd,jhd->htj", query_heads, key_heads, preferred_element_type=jnp.float32)
    causal = jnp.arange(rows)[:, None] >= jnp.arange(rows)[None, :]
    gap = cumulative.T[:, :, None] - cumulative.T[:, None, :]
    weight = jnp.where(causal[None], jnp.exp(-jnp.where(causal[None], gap, 0.0)), 0.0)
    weighted = (scores * weight).astype(jnp.bfloat16)
    inner = jnp.einsum("htj,jhd->thd", weighted, value_heads, preferred_element_type=jnp.float32)
    value_wide = value_heads.astype(jnp.float32)
    tail = jnp.exp(cumulative - cumulative[-1:])
    keys_tail = key_heads.astype(jnp.float32) * tail[:, :, None]
    local_state = jnp.einsum("jhd,jhe->hde", keys_tail, value_wide, precision=HIGH)
    shard_decay = jnp.exp(-cumulative[-1])
    decay_rows = jnp.broadcast_to(shard_decay[:, None, None], (heads_here, 1, HEAD_DIM))
    pad = jnp.zeros((heads_here, 7, HEAD_DIM), jnp.float32)
    packed = jnp.concatenate([local_state, decay_rows, pad], axis=1)
    incoming = exclusive_scan(packed, "ctx")
    query_decayed = query_heads.astype(jnp.float32) * jnp.exp(-cumulative)[:, :, None]
    outer = jnp.einsum("thd,hde->the", query_decayed, incoming, precision=HIGH)
    mixed = inner + outer
    mean_sq = jnp.mean(mixed * mixed, axis=-1, keepdims=True)
    gain_heads = head_gain.astype(jnp.float32).reshape(heads_here, HEAD_DIM)
    normed = (
        (mixed * lax.rsqrt(mean_sq + EPSILON) * gain_heads)
        .astype(jnp.bfloat16)
        .reshape(rows, heads_here * HEAD_DIM)
    )
    width = residual.shape[1]
    full = width * groups
    weight_all = lax.all_gather(out_weight, "ctx", axis=0, tiled=True).reshape(
        groups, width, heads_here * HEAD_DIM
    )
    partial_proj = jnp.einsum(
        "tk,gck->gtc", normed, weight_all, preferred_element_type=jnp.float32
    ).astype(jnp.bfloat16)
    total = lax.psum_scatter(partial_proj, "head", scatter_dimension=0, tiled=True)
    stream_mine = residual.astype(jnp.float32) + total[0].astype(jnp.float32)
    sq_part = jnp.sum(stream_mine * stream_mine, axis=1)
    sq_hi = sq_part.astype(jnp.bfloat16)
    sq_lo = (sq_part - sq_hi.astype(jnp.float32)).astype(jnp.bfloat16)
    experts = router.shape[1]
    capacity = 3 * rows * TOP // (2 * experts)
    lane = 128
    wide = width + lane
    other_id = expert_ids[:, ::-1].astype(jnp.bfloat16)
    token_rows = jnp.concatenate(
        [
            stream_mine.astype(jnp.bfloat16),
            sq_hi[:, None],
            sq_lo[:, None],
            jnp.zeros((rows, lane - 2), jnp.bfloat16),
        ],
        axis=1,
    )
    token_rows = jnp.concatenate([token_rows, jnp.zeros((8, wide), jnp.bfloat16)], axis=0)
    flat_ids = expert_ids.reshape(-1)
    onehot = (flat_ids[:, None] == jnp.arange(experts, dtype=jnp.int32)[None, :]).astype(jnp.int32)
    before = jnp.cumsum(onehot, axis=0) - onehot
    position = jnp.sum(before * onehot, axis=1)
    slot = flat_ids * capacity + position
    owner = jnp.arange(rows * TOP, dtype=jnp.int32) // TOP
    slot_token = jnp.full((experts * capacity,), rows, jnp.int32).at[slot].set(owner)
    slot_other = jnp.zeros((experts * capacity,), jnp.bfloat16).at[slot].set(other_id.reshape(-1))
    outgoing = token_rows[slot_token]
    outgoing = outgoing.at[:, width + 2].set(slot_other).reshape(experts, capacity, wide)
    arriving = lax.all_to_all(outgoing, "ctx", split_axis=0, concat_axis=0, tiled=True)
    flat = arriving.reshape(-1, wide)
    slots_here = flat.shape[0]
    sq_rows = jnp.transpose(flat[:, width:width + 2]).reshape(2 * slots_here // width, width)
    spare = 7 - sq_rows.shape[0]
    extra = jnp.concatenate(
        [norm_gain[None, :], sq_rows, jnp.zeros((spare, width), jnp.bfloat16)], axis=0
    )
    gathered = lax.all_gather(jnp.concatenate([flat[:, :width], extra], axis=0), "head", axis=0)
    stream_blocks = gathered[:, :slots_here].astype(jnp.float32)
    gain_blocks = gathered[:, slots_here].astype(jnp.float32)
    sq_parts = gathered[:, slots_here + 1 : slots_here + 1 + sq_rows.shape[0]].astype(jnp.float32)
    sq_parts = sq_parts.reshape(groups, 2, slots_here)
    stream_sq = jnp.sum(sq_parts, axis=(0, 1))[None, :, None] / full
    other_here = flat[:, width + 2].astype(jnp.int32)
    moe_in = (stream_blocks * lax.rsqrt(stream_sq + EPSILON) * gain_blocks[:, None, :]).astype(
        jnp.bfloat16
    )
    router_blocks = router.reshape(groups, width, router.shape[1])
    logits = jnp.einsum("grc,gce->re", moe_in, router_blocks, preferred_element_type=jnp.float32)
    expert_here = lax.axis_index("ctx")
    names = jnp.arange(experts, dtype=jnp.int32)[None, :]
    own_logit = jnp.sum(jnp.where(names == expert_here, logits, 0.0), axis=1)
    other_logit = jnp.sum(jnp.where(names == other_here[:, None], logits, 0.0), axis=1)
    mix_here = jax.nn.sigmoid(own_logit - other_logit)
    mix_hi = mix_here.astype(jnp.bfloat16)
    mix_lo = (mix_here - mix_hi.astype(jnp.float32)).astype(jnp.bfloat16)
    hidden = gate_weight.shape[2]
    gate = jnp.einsum(
        "grc,gcf->rf", moe_in, gate_weight[0].reshape(groups, width, hidden),
        preferred_element_type=jnp.float32,
    )
    up = jnp.einsum(
        "grc,gcf->rf", moe_in, up_weight[0].reshape(groups, width, hidden),
        preferred_element_type=jnp.float32,
    )
    activated = (jax.nn.silu(gate) * up).astype(jnp.bfloat16)
    down = down_weight[0].reshape(down_weight.shape[1], groups, width)
    partial_value = jnp.einsum(
        "rf,fgc->grc", activated, down, preferred_element_type=jnp.float32
    ).astype(jnp.bfloat16)
    summed = lax.psum_scatter(partial_value, "head", scatter_dimension=0, tiled=True)[0]
    back = jnp.concatenate(
        [
            summed,
            mix_hi[:, None],
            mix_lo[:, None],
            jnp.zeros((slots_here, lane - 2), jnp.bfloat16),
        ],
        axis=1,
    ).reshape(arriving.shape[0], arriving.shape[1], wide)
    returned = lax.all_to_all(back, "ctx", split_axis=0, concat_axis=0, tiled=True)
    picked_rows = returned.reshape(experts * capacity, wide)[slot].astype(jnp.float32)
    picked_rows = picked_rows.reshape(rows, TOP, wide)
    mix_weights = picked_rows[:, :, width] + picked_rows[:, :, width + 1]
    moe_out = jnp.sum(picked_rows[:, :, :width] * mix_weights[:, :, None], axis=1)
    return stream_mine + moe_out


def solution(mesh):
    placed = (
        P("ctx", "head"),
        P("ctx", "head"),
        P("ctx", "head"),
        P("ctx", "head"),
        P("head"),
        P("ctx", "head"),
        P("ctx", "head"),
        P("head"),
        P(),
        P("ctx", None),
        P("ctx", None, "head"),
        P("ctx", None, "head"),
        P("ctx", "head", None),
    )
    return jax.shard_map(
        on_device, mesh=mesh, in_specs=placed, out_specs=P("ctx", "head"), check_vma=False
    )
```
